256 devices in a mesh: space: 64 (over x_hi, y, z), dp: 4 (over x_lo, core).
Axes of the slice: x: 4 (x_hi: 2, x_lo: 2; x = x_hi * 2 + x_lo), y: 4, z: 8, core: 2. Of those that a mesh axis runs over, the one named last changes fastest.
Arguments:
- input_states: bfloat16 [4, 64, 200, 1024], P('dp', 'space'), may hold values from -6 to 6
- loss_sensitivity: bfloat16 [4, 64, 200, 1024], P('dp', 'space'), may hold values from -6 to 6
- ocean: int32 [64, 1024], P('space'), may hold values 0 or 1
- neighbours: int32 [64, 8], P('space'), may hold values from -1 to 63, as said below
- fold_flag: int32 [64], P('space'), may hold values from 0 to 1, as said below
- w_first: bfloat16 [9, 200, 200], replicated, may hold values from -0.125 to 0.125
- w_second: bfloat16 [9, 200, 200], replicated, may hold values from -0.125 to 0.125
Outputs:
- prediction: bfloat16 [4, 64, 200, 1024], P('dp', 'space')
- earlier_kernel_slope: float32 [9, 200, 200], replicated
- latter_kernel_slope: float32 [9, 200, 200], replicated
The draws below stay inside these ranges and needn't reach their ends.
Inputs may be any that keep to these rules, and one draw needn't show every extreme that they name: Tiles sit on a grid of 6 x 16 tile positions, some of them land; the ocean tiles carry numbers 0 to 63 in no particular order of positions; longitude wraps; the top row's northern neighbour is the mirrored tile of the same row (fold_flag 1) and its diagonal northern neighbours are -1. The relation is symmetric: if u is t's neighbour in one direction, t is u's in the opposite one (north for north across the fold). `fold_flag`: 1 exactly for tiles of the top tile row.
All inputs are finite; a program needn't handle non-finite values. No bound on the sum of `ocean` on one device may be relied on, other than what follows from the above.
Results may differ from the reference program's by a relative error of at most 0.005.
Values may be sent and summed in bfloat16 or wider, within the bound.
No kernel may reach another device: no remote copies, remote signals or barrier semaphores. Data moves between devices by JAX's collectives and lax.ppermute only.
A program may use at most 64 MiB of HBM per device.

```python
import jax
import jax.numpy as jnp
from jax import lax

CH = 200
SIDE = 32
GRID_COLS = 16
TILES = 64
GRID_ROWS = 6
N_DP = 4


def tile_layout(key):
    rows = GRID_ROWS
    cols = GRID_COLS
    total = rows * cols
    order = jax.random.permutation(jax.random.fold_in(key, 11), total)
    ranking = jnp.zeros((total,), jnp.int32).at[order].set(jnp.arange(total, dtype=jnp.int32))
    ocean_pos = (ranking < TILES).astype(jnp.int32)
    tile_of_pos = jnp.where(ocean_pos == 1, jnp.cumsum(ocean_pos) - 1, -1).astype(jnp.int32)
    position = jnp.argsort(1 - ocean_pos, stable=True)[:TILES].astype(jnp.int32)
    row = position // cols
    col = position % cols
    top = row == rows - 1

    def lookup(r, c, allowed):
        spot = jnp.clip(r * cols + c % cols, 0, total - 1)
        return jnp.where(allowed, tile_of_pos[spot], -1)
    everywhere = jnp.ones_like(top)
    north = jnp.where(top, lookup(row, cols - 1 - col, everywhere), lookup(row + 1, col, everywhere))
    south = lookup(row - 1, col, row >= 1)
    east = lookup(row, col + 1, everywhere)
    west = lookup(row, col - 1 + cols, everywhere)
    north_east = lookup(row + 1, col + 1, jnp.logical_not(top))
    north_west = lookup(row + 1, col - 1 + cols, jnp.logical_not(top))
    south_east = lookup(row - 1, col + 1, row >= 1)
    south_west = lookup(row - 1, col - 1 + cols, row >= 1)
    table = jnp.stack([north, south, east, west, north_east, north_west, south_east, south_west], axis=1).astype(jnp.int32)
    relabel = jax.random.permutation(jax.random.fold_in(key, 23), TILES).astype(jnp.int32)
    mapped = jnp.where(table >= 0, relabel[jnp.maximum(table, 0)], -1).astype(jnp.int32)
    new_table = jnp.zeros((TILES, 8), jnp.int32).at[relabel].set(mapped)
    new_flag = jnp.zeros((TILES,), jnp.int32).at[relabel].set(top.astype(jnp.int32))
    return (new_table, new_flag)


def draw_neighbours(key, part):
    return tile_layout(key)[0]


def draw_fold_flag(key, part):
    return tile_layout(key)[1]


def set_ends(drawn, stream_key, least, high):
    shape = drawn.shape
    index_at = [jax.random.randint(jax.random.fold_in(stream_key, axis), (), 0, shape[axis]) for axis in range(len(shape))]
    drawn = drawn.at[tuple(index_at)].set(least)
    longest = shape.index(max(shape))
    index_at[longest] = (index_at[longest] + 1) % shape[longest]
    return drawn.at[tuple(index_at)].set(high)


def block_levels(stream_key, dims, pieces, least, top_value):
    def one(dim, blocks):
        heights = jax.random.uniform(jax.random.fold_in(jax.random.fold_in(stream_key, 6), dim), (blocks,), jnp.float32, least / len(pieces), top_value / len(pieces))
        return jnp.repeat(jnp.exp(heights), dims[dim] // blocks).reshape((-1,) + (1,) * (len(dims) - dim - 1))

    factor_of = one(*pieces[0])
    for cut in pieces[1:]:
        factor_of = factor_of * one(*cut)
    return factor_of


def normal_values(stream_key, shape, spread, bound, cuts=(), held_as=jnp.bfloat16):
    factor_of = block_levels(stream_key, shape, cuts, -0.22, 0.18) if cuts else 1.0
    array = jax.random.normal(stream_key, shape, jnp.float32) * spread * factor_of
    return jnp.minimum(jnp.maximum(array, -bound), bound).astype(held_as)


def setup_inputs(seed: int = 0) -> dict:
    splits = jax.random.split(jax.random.key(seed), 8)
    return {
        "input_states": normal_values(splits[0], (N_DP, TILES, CH, SIDE * SIDE), 1.0, 6.0, ((0, 4), (1, 64))),
        "loss_sensitivity": normal_values(splits[1], (N_DP, TILES, CH, SIDE * SIDE), 1.0, 6.0, ((0, 4), (1, 64))),
        "ocean": set_ends((jax.random.randint(splits[2], (TILES, SIDE * SIDE), 0, 8) < 7).astype(jnp.int32), jax.random.fold_in(splits[2], 1), 0, 1),
        "neighbours": draw_neighbours(jax.random.fold_in(splits[7], 71), 0),
        "fold_flag": draw_fold_flag(jax.random.fold_in(splits[7], 71), 0),
        "w_first": normal_values(splits[5], (9, CH, CH), (9 * CH) ** -0.5, 0.125),
        "w_second": normal_values(splits[6], (9, CH, CH), (9 * CH) ** -0.5, 0.125),
    }


SQRT_TWO_PI = 0.7978845608028654
CUBIC = 0.044715

def gelu_pair(a):
    inner = SQRT_TWO_PI * (a + CUBIC * a * a * a)
    tangent = jnp.tanh(inner)
    value = 0.5 * a * (1.0 + tangent)
    slope = 0.5 * (1.0 + tangent) + 0.5 * a * (1.0 - tangent * tangent) * SQRT_TWO_PI * (1.0 + 3.0 * CUBIC * a * a)
    return (value, slope)

def pad_all(field, neighbours, fold_flag):
    patch_extent = field.shape[2]
    row_low = field[:, :, 0, :]
    row_high = field[:, :, patch_extent - 1, :]
    col_low = field[:, :, :, 0]
    col_high = field[:, :, :, patch_extent - 1]

    def pick(strip, k):
        index = neighbours[:, k]
        valid = (index >= 0).astype(jnp.float32)
        return strip[jnp.maximum(index, 0)] * valid[:, None, None]
    north = jnp.where((fold_flag == 1)[:, None, None], pick(row_high, 0)[:, :, ::-1], pick(row_low, 0))
    south = pick(row_high, 1)
    east = pick(col_low, 2)
    west = pick(col_high, 3)
    north_east = pick(row_low, 4)[:, :, 0:1]
    north_west = pick(row_low, 5)[:, :, patch_extent - 1:patch_extent]
    south_east = pick(row_high, 6)[:, :, 0:1]
    south_west = pick(row_high, 7)[:, :, patch_extent - 1:patch_extent]
    middle = jnp.concatenate([west[..., None], field, east[..., None]], axis=3)
    bottom = jnp.concatenate([south_west, south, south_east], axis=2)[:, :, None, :]
    top = jnp.concatenate([north_west, north, north_east], axis=2)[:, :, None, :]
    return jnp.concatenate([bottom, middle, top], axis=2)

def conv_ref(padded, weights):
    patch_extent = padded.shape[2] - 2
    total = jnp.zeros((padded.shape[0], weights.shape[1], patch_extent, patch_extent), jnp.float32)
    for k in range(9):
        shift_r = k // 3 - 1
        shift_c = k % 3 - 1
        window = padded[:, :, 1 + shift_r:1 + shift_r + patch_extent, 1 + shift_c:1 + shift_c + patch_extent]
        total = total + jnp.einsum('oi,tirc->torc', weights[k], window, precision=lax.Precision.HIGHEST)
    return total

def reference(input_states, loss_sensitivity, ocean, neighbours, fold_flag, w_first, w_second):
    patch_total = input_states.shape[1]
    feature_depth = input_states.shape[2]
    patch_extent = SIDE
    water_indicator = ocean.astype(jnp.float32).reshape(patch_total, 1, patch_extent, patch_extent)
    first = w_first.astype(jnp.float32)
    second = w_second.astype(jnp.float32)

    def solitary_bundle(pair):
        tiles, grads = pair
        inputs = tiles.astype(jnp.float32).reshape(patch_total, feature_depth, patch_extent, patch_extent)
        in_padded = pad_all(inputs, neighbours, fold_flag)
        pre_first = conv_ref(in_padded, first)
        value, slope = gelu_pair(pre_first)
        hidden = (value * water_indicator).astype(jnp.bfloat16)
        hidden = lax.optimization_barrier(hidden).astype(jnp.float32)

        def layer_two(weights, field):
            return conv_ref(pad_all(field, neighbours, fold_flag), weights)
        latter_linear_response, pull_two = jax.vjp(layer_two, second, hidden)
        prediction = (latter_linear_response * water_indicator).astype(jnp.bfloat16).reshape(patch_total, feature_depth, patch_extent * patch_extent)
        masked = grads.astype(jnp.float32).reshape(patch_total, feature_depth, patch_extent, patch_extent) * water_indicator
        latter_kernel_slope, back = pull_two(masked)
        pre_grad = (back * water_indicator * slope).astype(jnp.bfloat16)
        pre_grad = lax.optimization_barrier(pre_grad).astype(jnp.float32)
        _, pull_one = jax.vjp(lambda weights: conv_ref(in_padded, weights), first)
        earlier_kernel_slope, = pull_one(pre_grad)
        return (prediction, earlier_kernel_slope, latter_kernel_slope)
    prediction, earlier_kernel_slope, latter_kernel_slope = lax.map(solitary_bundle, (input_states, loss_sensitivity))
    return (prediction, lax.optimization_barrier(jnp.sum(earlier_kernel_slope, axis=0)), lax.optimization_barrier(jnp.sum(latter_kernel_slope, axis=0)))
```

```python
import jax
import jax.numpy as jnp
from jax import lax
from jax.sharding import PartitionSpec as P

SIDE = 32


SQRT_TWO_PI = 0.7978845608028654
CUBIC = 0.044715


def gelu_pair(a):
    inner = SQRT_TWO_PI * (a + CUBIC * a * a * a)
    tangent = jnp.tanh(inner)
    value = 0.5 * a * (1.0 + tangent)
    slope = 0.5 * (1.0 + tangent) + 0.5 * a * (1.0 - tangent * tangent) * SQRT_TWO_PI * (
        1.0 + 3.0 * CUBIC * a * a
    )
    return (value, slope)


def edge_strips(field):
    patch_extent = field.shape[2]
    return jnp.concatenate(
        [
            field[:, :, 0, :],
            field[:, :, patch_extent - 1, :],
            field[:, :, :, 0],
            field[:, :, :, patch_extent - 1],
        ],
        axis=2,
    )


def strip_parts(piece, neighbours, fold_flag):
    amount = piece.shape[0]
    patch_extent = piece.shape[2] // 4

    def pick(k):
        index = neighbours[:, k]
        valid = ((index >= 0) & (index < amount)).astype(piece.dtype)
        return jnp.take(piece, jnp.clip(index, 0, amount - 1), axis=0) * valid[:, None, None]

    from_north = pick(0)
    north = jnp.where(
        (fold_flag == 1)[:, None, None],
        from_north[:, :, patch_extent : 2 * patch_extent][:, :, ::-1],
        from_north[:, :, 0:patch_extent],
    )
    south = pick(1)[:, :, patch_extent : 2 * patch_extent]
    east = pick(2)[:, :, 2 * patch_extent : 3 * patch_extent]
    west = pick(3)[:, :, 3 * patch_extent : 4 * patch_extent]
    corners = jnp.stack(
        [
            pick(4)[:, :, 0],
            pick(5)[:, :, patch_extent - 1],
            pick(6)[:, :, patch_extent],
            pick(7)[:, :, 2 * patch_extent - 1],
        ],
        axis=-1,
    )
    return (north, south, east, west, corners)


def collect_rims(strips, neighbours, fold_flag):
    found = strip_parts(lax.all_gather(strips, "space", axis=0, tiled=True), neighbours, fold_flag)
    return tuple((b for b in found))


def collect_two_rims(first, second, neighbours, fold_flag):
    depth = first.shape[1]
    gathered = lax.all_gather(jnp.concatenate([first, second], axis=1), "space", axis=0, tiled=True)
    return (
        strip_parts(gathered[:, :depth], neighbours, fold_flag),
        strip_parts(gathered[:, depth:], neighbours, fold_flag),
    )


REDUCE_AXES = ("space", "dp")


def all_sum(x, mesh_sizes):
    n = mesh_sizes
    nbits = n.bit_length() - 1
    idx = lax.axis_index(REDUCE_AXES)
    buf = x.reshape(-1)
    size = buf.shape[0]
    padded = -(-size // n) * n
    buf = jnp.pad(buf, (0, padded - size))
    for b in range(nbits):
        half = buf.shape[0] // 2
        me = (idx >> b) & 1
        pairs = [(i, i ^ (1 << b)) for i in range(n)]
        keep = lax.dynamic_slice(buf, (me * half,), (half,))
        send = lax.dynamic_slice(buf, ((1 - me) * half,), (half,))
        buf = keep + lax.ppermute(send, REDUCE_AXES, pairs)
    for b in reversed(range(nbits)):
        me = (idx >> b) & 1
        pairs = [(i, i ^ (1 << b)) for i in range(n)]
        recv = lax.ppermute(buf, REDUCE_AXES, pairs)
        buf = jnp.concatenate([jnp.where(me == 0, buf, recv), jnp.where(me == 0, recv, buf)])
    return buf[:size].reshape(x.shape)


def padded_tiles(field, parts):
    north, south, east, west, corners = parts
    middle = jnp.concatenate([west[..., None], field, east[..., None]], axis=3)
    bottom = jnp.concatenate([corners[:, :, 3:4], south, corners[:, :, 2:3]], axis=2)[:, :, None, :]
    top = jnp.concatenate([corners[:, :, 1:2], north, corners[:, :, 0:1]], axis=2)[:, :, None, :]
    return jnp.concatenate([bottom, middle, top], axis=2)


def window(padded, shift_r, shift_c):
    patch_extent = padded.shape[2] - 2
    part = padded[
        :, :, 1 + shift_r : 1 + shift_r + patch_extent, 1 + shift_c : 1 + shift_c + patch_extent
    ]
    return part.reshape(padded.shape[0], padded.shape[1], patch_extent * patch_extent)


def conv_forward(padded, weights):
    total = None
    for k in range(9):
        term = jnp.einsum(
            "oi,tic->toc",
            weights[k],
            window(padded, k // 3 - 1, k % 3 - 1),
            preferred_element_type=jnp.float32,
        )
        total = term if total is None else total + term
    return total


def conv_adjoint(padded, weights):
    total = None
    for k in range(9):
        term = jnp.einsum(
            "oi,toc->tic",
            weights[k],
            window(padded, 1 - k // 3, 1 - k % 3),
            preferred_element_type=jnp.float32,
        )
        total = term if total is None else total + term
    return total


def weight_grad(grads, padded):
    return jnp.stack(
        [
            jnp.einsum(
                "toc,tic->oi",
                grads,
                window(padded, k // 3 - 1, k % 3 - 1),
                preferred_element_type=jnp.float32,
            )
            for k in range(9)
        ],
        axis=0,
    )


def body(input_states, loss_sensitivity, ocean, neighbours, fold_flag, w_first, w_second):
    tiles = input_states[0]
    patch_total, feature_depth, cells = tiles.shape
    patch_extent = SIDE
    inputs = tiles.reshape(patch_total, feature_depth, patch_extent, patch_extent)
    water_indicator = ocean.astype(jnp.float32)[:, None, :]
    masked_grad = (loss_sensitivity[0].astype(jnp.float32) * water_indicator).astype(jnp.bfloat16)
    grad_tiles = masked_grad.reshape(patch_total, feature_depth, patch_extent, patch_extent)
    field_parts, grad_parts = collect_two_rims(
        edge_strips(inputs), edge_strips(grad_tiles), neighbours, fold_flag
    )
    in_padded = padded_tiles(inputs, field_parts)
    pre_first = conv_forward(in_padded, w_first)
    value, slope = gelu_pair(pre_first)
    hidden = (value * water_indicator).astype(jnp.bfloat16)
    hidden_tiles = hidden.reshape(patch_total, feature_depth, patch_extent, patch_extent)
    hidden_parts = collect_rims(edge_strips(hidden_tiles), neighbours, fold_flag)
    hidden_padded = padded_tiles(hidden_tiles, hidden_parts)
    latter_linear_response = conv_forward(hidden_padded, w_second)
    prediction = (latter_linear_response * water_indicator).astype(jnp.bfloat16)[None]
    grad_padded = padded_tiles(grad_tiles, grad_parts)
    latter_kernel_slope = weight_grad(masked_grad, hidden_padded)
    back = conv_adjoint(grad_padded, w_second).reshape(
        patch_total, feature_depth, patch_extent, patch_extent
    )
    top_row = grad_padded[:, :, patch_extent + 1, :]
    correction = jnp.zeros((patch_total, feature_depth, patch_extent), jnp.float32)
    for shift_c in (-1, 0, 1):
        segment = top_row[:, :, 1 - shift_c : 1 - shift_c + patch_extent]
        correction = correction + jnp.einsum(
            "oi,toc->tic", w_second[7 - shift_c], segment, preferred_element_type=jnp.float32
        )
        correction = correction - jnp.einsum(
            "oi,toc->tic", w_second[1 + shift_c], segment, preferred_element_type=jnp.float32
        )
    flipped = (fold_flag == 1).astype(jnp.float32)[:, None, None]
    back = back.at[:, :, patch_extent - 1, :].add(correction * flipped)
    pre_grad = (back.reshape(patch_total, feature_depth, cells) * water_indicator * slope).astype(
        jnp.bfloat16
    )
    earlier_kernel_slope = weight_grad(pre_grad, in_padded)
    devices = lax.psum(1, REDUCE_AXES)
    earlier_kernel_slope = all_sum(earlier_kernel_slope, devices)
    latter_kernel_slope = all_sum(latter_kernel_slope, devices)
    return (prediction, earlier_kernel_slope, latter_kernel_slope)


def solution(mesh):
    placed = (
        P("dp", "space", None, None),
        P("dp", "space", None, None),
        P("space", None),
        P("space", None),
        P("space"),
        P(),
        P(),
    )
    return jax.shard_map(
        body,
        mesh=mesh,
        in_specs=placed,
        out_specs=(P("dp", "space", None, None), P(), P()),
        check_vma=False,
    )
```

```python
import jax
import jax.numpy as jnp
from jax import lax
from jax.sharding import PartitionSpec as P

SIDE = 32


SQRT_TWO_PI = 0.7978845608028654
CUBIC = 0.044715


def gelu_pair(a):
    inner = SQRT_TWO_PI * (a + CUBIC * a * a * a)
    tangent = jnp.tanh(inner)
    value = 0.5 * a * (1.0 + tangent)
    slope = 0.5 * (1.0 + tangent) + 0.5 * a * (1.0 - tangent * tangent) * SQRT_TWO_PI * (
        1.0 + 3.0 * CUBIC * a * a
    )
    return (value, slope)


def edge_strips(field):
    patch_extent = field.shape[2]
    return jnp.concatenate(
        [
            field[:, :, 0, :],
            field[:, :, patch_extent - 1, :],
            field[:, :, :, 0],
            field[:, :, :, patch_extent - 1],
        ],
        axis=2,
    )


def strip_parts(piece, neighbours, fold_flag):
    amount = piece.shape[0]
    patch_extent = piece.shape[2] // 4

    def pick(k):
        index = neighbours[:, k]
        valid = ((index >= 0) & (index < amount)).astype(piece.dtype)
        return jnp.take(piece, jnp.clip(index, 0, amount - 1), axis=0) * valid[:, None, None]

    from_north = pick(0)
    north = jnp.where(
        (fold_flag == 1)[:, None, None],
        from_north[:, :, patch_extent : 2 * patch_extent][:, :, ::-1],
        from_north[:, :, 0:patch_extent],
    )
    south = pick(1)[:, :, patch_extent : 2 * patch_extent]
    east = pick(2)[:, :, 2 * patch_extent : 3 * patch_extent]
    west = pick(3)[:, :, 3 * patch_extent : 4 * patch_extent]
    corners = jnp.stack(
        [
            pick(4)[:, :, 0],
            pick(5)[:, :, patch_extent - 1],
            pick(6)[:, :, patch_extent],
            pick(7)[:, :, 2 * patch_extent - 1],
        ],
        axis=-1,
    )
    return (north, south, east, west, corners)


def collect_rims(strips, neighbours, fold_flag):
    found = strip_parts(lax.all_gather(strips, "space", axis=0, tiled=True), neighbours, fold_flag)
    return tuple((b for b in found))


def collect_two_rims(first, second, neighbours, fold_flag):
    depth = first.shape[1]
    gathered = lax.all_gather(jnp.concatenate([first, second], axis=1), "space", axis=0, tiled=True)
    return (
        strip_parts(gathered[:, :depth], neighbours, fold_flag),
        strip_parts(gathered[:, depth:], neighbours, fold_flag),
    )


REDUCE_AXES = ("space", "dp")


def all_sum(x, devices):
    digits = 0
    while 4 ** digits < devices:
        digits += 1
    idx = lax.axis_index(REDUCE_AXES)
    buf = x.reshape(-1, x.shape[-1])
    rows = buf.shape[0]
    unit = devices * 8
    buf = jnp.pad(buf, ((0, -(-rows // unit) * unit - rows), (0, 0)))
    for g in range(digits):
        quarter = buf.shape[0] // 4
        mine = (idx >> (2 * g)) & 3
        total = lax.dynamic_slice_in_dim(buf, mine * quarter, quarter, axis=0)
        for j in (1, 2, 3):
            pairs = [(i, i ^ (j << (2 * g))) for i in range(devices)]
            piece = lax.dynamic_slice_in_dim(buf, (mine ^ j) * quarter, quarter, axis=0)
            total = total + lax.ppermute(piece, REDUCE_AXES, pairs)
        buf = total
    for g in reversed(range(digits)):
        mine = (idx >> (2 * g)) & 3
        got = [buf]
        for j in (1, 2, 3):
            pairs = [(i, i ^ (j << (2 * g))) for i in range(devices)]
            got.append(lax.ppermute(buf, REDUCE_AXES, pairs))
        parts = []
        for p in range(4):
            rel = mine ^ p
            part = got[3]
            for j in (2, 1, 0):
                part = jnp.where(rel == j, got[j], part)
            parts.append(part)
        buf = jnp.concatenate(parts, axis=0)
    return buf[:rows].reshape(x.shape)


def padded_tiles(field, parts):
    north, south, east, west, corners = parts
    middle = jnp.concatenate([west[..., None], field, east[..., None]], axis=3)
    bottom = jnp.concatenate([corners[:, :, 3:4], south, corners[:, :, 2:3]], axis=2)[:, :, None, :]
    top = jnp.concatenate([corners[:, :, 1:2], north, corners[:, :, 0:1]], axis=2)[:, :, None, :]
    return jnp.concatenate([bottom, middle, top], axis=2)


def window(padded, shift_r, shift_c):
    patch_extent = padded.shape[2] - 2
    part = padded[
        :, :, 1 + shift_r : 1 + shift_r + patch_extent, 1 + shift_c : 1 + shift_c + patch_extent
    ]
    return part.reshape(padded.shape[0], padded.shape[1], patch_extent * patch_extent)


def conv_forward(padded, weights):
    total = None
    for k in range(9):
        term = jnp.einsum(
            "oi,tic->toc",
            weights[k],
            window(padded, k // 3 - 1, k % 3 - 1),
            preferred_element_type=jnp.float32,
        )
        total = term if total is None else total + term
    return total


def conv_adjoint(padded, weights):
    total = None
    for k in range(9):
        term = jnp.einsum(
            "oi,toc->tic",
            weights[k],
            window(padded, 1 - k // 3, 1 - k % 3),
            preferred_element_type=jnp.float32,
        )
        total = term if total is None else total + term
    return total


def weight_grad(grads, padded):
    return jnp.stack(
        [
            jnp.einsum(
                "toc,tic->oi",
                grads,
                window(padded, k // 3 - 1, k % 3 - 1),
                preferred_element_type=jnp.float32,
            )
            for k in range(9)
        ],
        axis=0,
    )


def body(input_states, loss_sensitivity, ocean, neighbours, fold_flag, w_first, w_second):
    tiles = input_states[0]
    patch_total, feature_depth, cells = tiles.shape
    patch_extent = SIDE
    inputs = tiles.reshape(patch_total, feature_depth, patch_extent, patch_extent)
    water_indicator = ocean.astype(jnp.float32)[:, None, :]
    masked_grad = (loss_sensitivity[0].astype(jnp.float32) * water_indicator).astype(jnp.bfloat16)
    grad_tiles = masked_grad.reshape(patch_total, feature_depth, patch_extent, patch_extent)
    field_parts, grad_parts = collect_two_rims(
        edge_strips(inputs), edge_strips(grad_tiles), neighbours, fold_flag
    )
    in_padded = padded_tiles(inputs, field_parts)
    pre_first = conv_forward(in_padded, w_first)
    value, slope = gelu_pair(pre_first)
    hidden = (value * water_indicator).astype(jnp.bfloat16)
    hidden_tiles = hidden.reshape(patch_total, feature_depth, patch_extent, patch_extent)
    hidden_parts = collect_rims(edge_strips(hidden_tiles), neighbours, fold_flag)
    hidden_padded = padded_tiles(hidden_tiles, hidden_parts)
    latter_linear_response = conv_forward(hidden_padded, w_second)
    prediction = (latter_linear_response * water_indicator).astype(jnp.bfloat16)[None]
    grad_padded = padded_tiles(grad_tiles, grad_parts)
    latter_kernel_slope = weight_grad(masked_grad, hidden_padded)
    back = conv_adjoint(grad_padded, w_second).reshape(
        patch_total, feature_depth, patch_extent, patch_extent
    )
    top_row = grad_padded[:, :, patch_extent + 1, :]
    correction = jnp.zeros((patch_total, feature_depth, patch_extent), jnp.float32)
    for shift_c in (-1, 0, 1):
        segment = top_row[:, :, 1 - shift_c : 1 - shift_c + patch_extent]
        correction = correction + jnp.einsum(
            "oi,toc->tic", w_second[7 - shift_c], segment, preferred_element_type=jnp.float32
        )
        correction = correction - jnp.einsum(
            "oi,toc->tic", w_second[1 + shift_c], segment, preferred_element_type=jnp.float32
        )
    flipped = (fold_flag == 1).astype(jnp.float32)[:, None, None]
    back = back.at[:, :, patch_extent - 1, :].add(correction * flipped)
    pre_grad = (back.reshape(patch_total, feature_depth, cells) * water_indicator * slope).astype(
        jnp.bfloat16
    )
    earlier_kernel_slope = weight_grad(pre_grad, in_padded)
    devices = lax.psum(1, REDUCE_AXES)
    earlier_kernel_slope = all_sum(earlier_kernel_slope, devices)
    latter_kernel_slope = all_sum(latter_kernel_slope, devices)
    return (prediction, earlier_kernel_slope, latter_kernel_slope)


def solution(mesh):
    placed = (
        P("dp", "space", None, None),
        P("dp", "space", None, None),
        P("space", None),
        P("space", None),
        P("space"),
        P(),
        P(),
    )
    return jax.shard_map(
        body,
        mesh=mesh,
        in_specs=placed,
        out_specs=(P("dp", "space", None, None), P(), P()),
        check_vma=False,
    )
```

```python
import jax
import jax.numpy as jnp
from jax import lax
from jax.sharding import PartitionSpec as P

SIDE = 32


SQRT_TWO_PI = 0.7978845608028654
CUBIC = 0.044715


def gelu_pair(a):
    inner = SQRT_TWO_PI * (a + CUBIC * a * a * a)
    tangent = jnp.tanh(inner)
    value = 0.5 * a * (1.0 + tangent)
    slope = 0.5 * (1.0 + tangent) + 0.5 * a * (1.0 - tangent * tangent) * SQRT_TWO_PI * (
        1.0 + 3.0 * CUBIC * a * a
    )
    return (value, slope)


def edge_strips(field):
    patch_extent = field.shape[2]
    return jnp.concatenate(
        [
            field[:, :, 0, :],
            field[:, :, patch_extent - 1, :],
            field[:, :, :, 0],
            field[:, :, :, patch_extent - 1],
        ],
        axis=2,
    )


def strip_parts(piece, neighbours, fold_flag):
    amount = piece.shape[0]
    patch_extent = piece.shape[2] // 4

    def pick(k):
        index = neighbours[:, k]
        valid = ((index >= 0) & (index < amount)).astype(piece.dtype)
        return jnp.take(piece, jnp.clip(index, 0, amount - 1), axis=0) * valid[:, None, None]

    from_north = pick(0)
    north = jnp.where(
        (fold_flag == 1)[:, None, None],
        from_north[:, :, patch_extent : 2 * patch_extent][:, :, ::-1],
        from_north[:, :, 0:patch_extent],
    )
    south = pick(1)[:, :, patch_extent : 2 * patch_extent]
    east = pick(2)[:, :, 2 * patch_extent : 3 * patch_extent]
    west = pick(3)[:, :, 3 * patch_extent : 4 * patch_extent]
    corners = jnp.stack(
        [
            pick(4)[:, :, 0],
            pick(5)[:, :, patch_extent - 1],
            pick(6)[:, :, patch_extent],
            pick(7)[:, :, 2 * patch_extent - 1],
        ],
        axis=-1,
    )
    return (north, south, east, west, corners)


def collect_rims(strips, neighbours, fold_flag):
    found = strip_parts(lax.all_gather(strips, "space", axis=0, tiled=True), neighbours, fold_flag)
    return tuple((b for b in found))


def collect_two_rims(first, second, neighbours, fold_flag):
    depth = first.shape[1]
    gathered = lax.all_gather(jnp.concatenate([first, second], axis=1), "space", axis=0, tiled=True)
    return (
        strip_parts(gathered[:, :depth], neighbours, fold_flag),
        strip_parts(gathered[:, depth:], neighbours, fold_flag),
    )


def exchange_rims(fields, neighbours, fold_flag):
    amount = lax.psum(1, "space")
    own = neighbours[0]
    dest = jnp.arange(amount, dtype=own.dtype)

    def toward(directions):
        hit = jnp.zeros((amount,), jnp.bool_)
        for k in directions:
            hit = hit | (own[k] == dest)
        return hit[:, None, None]

    up, down = toward((0, 4, 5)), toward((1, 6, 7))
    east, west = toward((2,)), toward((3,))
    slots = []
    for field in fields:
        extent = field.shape[2]
        row_low, row_high = field[0, :, 0, :], field[0, :, extent - 1, :]
        col_low, col_high = field[0, :, :, 0], field[0, :, :, extent - 1]
        empty = jnp.zeros_like(row_low)[None]
        slots.append(jnp.where(up, row_high[None], jnp.where(down, row_low[None], empty)))
        slots.append(jnp.where(east, col_high[None], jnp.where(west, col_low[None], empty)))
    got = lax.all_to_all(jnp.concatenate(slots, axis=2), "space", 0, 0, tiled=True)
    found = []
    for n, field in enumerate(fields):
        extent = field.shape[2]
        rows = got[:, :, 2 * n * extent : (2 * n + 1) * extent]
        cols = got[:, :, (2 * n + 1) * extent : (2 * n + 2) * extent]

        def pick(part, k):
            index = neighbours[:, k]
            valid = ((index >= 0) & (index < amount)).astype(part.dtype)
            return jnp.take(part, jnp.clip(index, 0, amount - 1), axis=0) * valid[:, None, None]

        from_north = pick(rows, 0)
        north = jnp.where((fold_flag == 1)[:, None, None], from_north[:, :, ::-1], from_north)
        corners = jnp.stack(
            [
                pick(rows, 4)[:, :, 0],
                pick(rows, 5)[:, :, extent - 1],
                pick(rows, 6)[:, :, 0],
                pick(rows, 7)[:, :, extent - 1],
            ],
            axis=-1,
        )
        found.append((north, pick(rows, 1), pick(cols, 2), pick(cols, 3), corners))
    return found


REDUCE_AXES = ("space", "dp")


def all_sum(x, mesh_sizes):
    n = mesh_sizes
    nbits = n.bit_length() - 1
    idx = lax.axis_index(REDUCE_AXES)
    buf = x.reshape(-1)
    size = buf.shape[0]
    padded = -(-size // n) * n
    buf = jnp.pad(buf, (0, padded - size))
    for b in range(nbits):
        half = buf.shape[0] // 2
        me = (idx >> b) & 1
        pairs = [(i, i ^ (1 << b)) for i in range(n)]
        keep = lax.dynamic_slice(buf, (me * half,), (half,))
        send = lax.dynamic_slice(buf, ((1 - me) * half,), (half,))
        buf = keep + lax.ppermute(send, REDUCE_AXES, pairs)
    for b in reversed(range(nbits)):
        me = (idx >> b) & 1
        pairs = [(i, i ^ (1 << b)) for i in range(n)]
        recv = lax.ppermute(buf, REDUCE_AXES, pairs)
        buf = jnp.concatenate([jnp.where(me == 0, buf, recv), jnp.where(me == 0, recv, buf)])
    return buf[:size].reshape(x.shape)


def padded_tiles(field, parts):
    north, south, east, west, corners = parts
    middle = jnp.concatenate([west[..., None], field, east[..., None]], axis=3)
    bottom = jnp.concatenate([corners[:, :, 3:4], south, corners[:, :, 2:3]], axis=2)[:, :, None, :]
    top = jnp.concatenate([corners[:, :, 1:2], north, corners[:, :, 0:1]], axis=2)[:, :, None, :]
    return jnp.concatenate([bottom, middle, top], axis=2)


def window(padded, shift_r, shift_c):
    patch_extent = padded.shape[2] - 2
    part = padded[
        :, :, 1 + shift_r : 1 + shift_r + patch_extent, 1 + shift_c : 1 + shift_c + patch_extent
    ]
    return part.reshape(padded.shape[0], padded.shape[1], patch_extent * patch_extent)


def conv_forward(padded, weights):
    total = None
    for k in range(9):
        term = jnp.einsum(
            "oi,tic->toc",
            weights[k],
            window(padded, k // 3 - 1, k % 3 - 1),
            preferred_element_type=jnp.float32,
        )
        total = term if total is None else total + term
    return total


def conv_adjoint(padded, weights):
    total = None
    for k in range(9):
        term = jnp.einsum(
            "oi,toc->tic",
            weights[k],
            window(padded, 1 - k // 3, 1 - k % 3),
            preferred_element_type=jnp.float32,
        )
        total = term if total is None else total + term
    return total


def weight_grad(grads, padded):
    return jnp.stack(
        [
            jnp.einsum(
                "toc,tic->oi",
                grads,
                window(padded, k // 3 - 1, k % 3 - 1),
                preferred_element_type=jnp.float32,
            )
            for k in range(9)
        ],
        axis=0,
    )


def body(input_states, loss_sensitivity, ocean, neighbours, fold_flag, w_first, w_second):
    tiles = input_states[0]
    patch_total, feature_depth, cells = tiles.shape
    patch_extent = SIDE
    inputs = tiles.reshape(patch_total, feature_depth, patch_extent, patch_extent)
    water_indicator = ocean.astype(jnp.float32)[:, None, :]
    masked_grad = (loss_sensitivity[0].astype(jnp.float32) * water_indicator).astype(jnp.bfloat16)
    grad_tiles = masked_grad.reshape(patch_total, feature_depth, patch_extent, patch_extent)
    field_parts, grad_parts = exchange_rims((inputs, grad_tiles), neighbours, fold_flag)
    in_padded = padded_tiles(inputs, field_parts)
    pre_first = conv_forward(in_padded, w_first)
    value, slope = gelu_pair(pre_first)
    hidden = (value * water_indicator).astype(jnp.bfloat16)
    hidden_tiles = hidden.reshape(patch_total, feature_depth, patch_extent, patch_extent)
    (hidden_parts,) = exchange_rims((hidden_tiles,), neighbours, fold_flag)
    hidden_padded = padded_tiles(hidden_tiles, hidden_parts)
    latter_linear_response = conv_forward(hidden_padded, w_second)
    prediction = (latter_linear_response * water_indicator).astype(jnp.bfloat16)[None]
    grad_padded = padded_tiles(grad_tiles, grad_parts)
    latter_kernel_slope = weight_grad(masked_grad, hidden_padded)
    back = conv_adjoint(grad_padded, w_second).reshape(
        patch_total, feature_depth, patch_extent, patch_extent
    )
    top_row = grad_padded[:, :, patch_extent + 1, :]
    correction = jnp.zeros((patch_total, feature_depth, patch_extent), jnp.float32)
    for shift_c in (-1, 0, 1):
        segment = top_row[:, :, 1 - shift_c : 1 - shift_c + patch_extent]
        correction = correction + jnp.einsum(
            "oi,toc->tic", w_second[7 - shift_c], segment, preferred_element_type=jnp.float32
        )
        correction = correction - jnp.einsum(
            "oi,toc->tic", w_second[1 + shift_c], segment, preferred_element_type=jnp.float32
        )
    flipped = (fold_flag == 1).astype(jnp.float32)[:, None, None]
    back = back.at[:, :, patch_extent - 1, :].add(correction * flipped)
    pre_grad = (back.reshape(patch_total, feature_depth, cells) * water_indicator * slope).astype(
        jnp.bfloat16
    )
    earlier_kernel_slope = weight_grad(pre_grad, in_padded)
    devices = lax.psum(1, REDUCE_AXES)
    earlier_kernel_slope = all_sum(earlier_kernel_slope, devices)
    latter_kernel_slope = all_sum(latter_kernel_slope, devices)
    return (prediction, earlier_kernel_slope, latter_kernel_slope)


def solution(mesh):
    placed = (
        P("dp", "space", None, None),
        P("dp", "space", None, None),
        P("space", None),
        P("space", None),
        P("space"),
        P(),
        P(),
    )
    return jax.shard_map(
        body,
        mesh=mesh,
        in_specs=placed,
        out_specs=(P("dp", "space", None, None), P(), P()),
        check_vma=False,
    )
```

```python
import jax
import jax.numpy as jnp
from jax import lax
from jax.sharding import PartitionSpec as P

SIDE = 32


SQRT_TWO_PI = 0.7978845608028654
CUBIC = 0.044715


def gelu_pair(a):
    inner = SQRT_TWO_PI * (a + CUBIC * a * a * a)
    tangent = jnp.tanh(inner)
    value = 0.5 * a * (1.0 + tangent)
    slope = 0.5 * (1.0 + tangent) + 0.5 * a * (1.0 - tangent * tangent) * SQRT_TWO_PI * (
        1.0 + 3.0 * CUBIC * a * a
    )
    return (value, slope)


def edge_strips(field):
    patch_extent = field.shape[2]
    return jnp.concatenate(
        [
            field[:, :, 0, :],
            field[:, :, patch_extent - 1, :],
            field[:, :, :, 0],
            field[:, :, :, patch_extent - 1],
        ],
        axis=2,
    )


def strip_parts(piece, neighbours, fold_flag):
    amount = piece.shape[0]
    patch_extent = piece.shape[2] // 4

    def pick(k):
        index = neighbours[:, k]
        valid = ((index >= 0) & (index < amount)).astype(piece.dtype)
        return jnp.take(piece, jnp.clip(index, 0, amount - 1), axis=0) * valid[:, None, None]

    from_north = pick(0)
    north = jnp.where(
        (fold_flag == 1)[:, None, None],
        from_north[:, :, patch_extent : 2 * patch_extent][:, :, ::-1],
        from_north[:, :, 0:patch_extent],
    )
    south = pick(1)[:, :, patch_extent : 2 * patch_extent]
    east = pick(2)[:, :, 2 * patch_extent : 3 * patch_extent]
    west = pick(3)[:, :, 3 * patch_extent : 4 * patch_extent]
    corners = jnp.stack(
        [
            pick(4)[:, :, 0],
            pick(5)[:, :, patch_extent - 1],
            pick(6)[:, :, patch_extent],
            pick(7)[:, :, 2 * patch_extent - 1],
        ],
        axis=-1,
    )
    return (north, south, east, west, corners)


def collect_rims(strips, neighbours, fold_flag):
    found = strip_parts(lax.all_gather(strips, "space", axis=0, tiled=True), neighbours, fold_flag)
    return tuple((b for b in found))


def collect_two_rims(first, second, neighbours, fold_flag):
    depth = first.shape[1]
    gathered = lax.all_gather(jnp.concatenate([first, second], axis=1), "space", axis=0, tiled=True)
    return (
        strip_parts(gathered[:, :depth], neighbours, fold_flag),
        strip_parts(gathered[:, depth:], neighbours, fold_flag),
    )


def exchange_rims(fields, neighbours, fold_flag):
    amount = lax.psum(1, "space")
    own = neighbours[0]
    dest = jnp.arange(amount, dtype=own.dtype)

    def toward(directions):
        hit = jnp.zeros((amount,), jnp.bool_)
        for k in directions:
            hit = hit | (own[k] == dest)
        return hit[:, None, None]

    up, down = toward((0, 4, 5)), toward((1, 6, 7))
    east, west = toward((2,)), toward((3,))
    slots = []
    for field in fields:
        extent = field.shape[2]
        row_low, row_high = field[0, :, 0, :], field[0, :, extent - 1, :]
        col_low, col_high = field[0, :, :, 0], field[0, :, :, extent - 1]
        empty = jnp.zeros_like(row_low)[None]
        slots.append(jnp.where(up, row_high[None], jnp.where(down, row_low[None], empty)))
        slots.append(jnp.where(east, col_high[None], jnp.where(west, col_low[None], empty)))
    got = lax.all_to_all(jnp.concatenate(slots, axis=2), "space", 0, 0, tiled=True)
    found = []
    for n, field in enumerate(fields):
        extent = field.shape[2]
        rows = got[:, :, 2 * n * extent : (2 * n + 1) * extent]
        cols = got[:, :, (2 * n + 1) * extent : (2 * n + 2) * extent]

        def pick(part, k):
            index = neighbours[:, k]
            valid = ((index >= 0) & (index < amount)).astype(part.dtype)
            return jnp.take(part, jnp.clip(index, 0, amount - 1), axis=0) * valid[:, None, None]

        from_north = pick(rows, 0)
        north = jnp.where((fold_flag == 1)[:, None, None], from_north[:, :, ::-1], from_north)
        corners = jnp.stack(
            [
                pick(rows, 4)[:, :, 0],
                pick(rows, 5)[:, :, extent - 1],
                pick(rows, 6)[:, :, 0],
                pick(rows, 7)[:, :, extent - 1],
            ],
            axis=-1,
        )
        found.append((north, pick(rows, 1), pick(cols, 2), pick(cols, 3), corners))
    return found


REDUCE_AXES = ("space", "dp")


def all_sum(x, mesh_sizes):
    n = mesh_sizes
    nbits = n.bit_length() - 1
    idx = lax.axis_index(REDUCE_AXES)
    buf = x.reshape(-1)
    size = buf.shape[0]
    padded = -(-size // n) * n
    buf = jnp.pad(buf, (0, padded - size))
    for b in range(nbits):
        half = buf.shape[0] // 2
        me = (idx >> b) & 1
        pairs = [(i, i ^ (1 << b)) for i in range(n)]
        keep = lax.dynamic_slice(buf, (me * half,), (half,))
        send = lax.dynamic_slice(buf, ((1 - me) * half,), (half,))
        buf = keep + lax.ppermute(send, REDUCE_AXES, pairs)
    for b in reversed(range(nbits)):
        me = (idx >> b) & 1
        pairs = [(i, i ^ (1 << b)) for i in range(n)]
        recv = lax.ppermute(buf, REDUCE_AXES, pairs)
        buf = jnp.concatenate([jnp.where(me == 0, buf, recv), jnp.where(me == 0, recv, buf)])
    return buf[:size].reshape(x.shape)


def padded_tiles(field, parts):
    north, south, east, west, corners = parts
    middle = jnp.concatenate([west[..., None], field, east[..., None]], axis=3)
    bottom = jnp.concatenate([corners[:, :, 3:4], south, corners[:, :, 2:3]], axis=2)[:, :, None, :]
    top = jnp.concatenate([corners[:, :, 1:2], north, corners[:, :, 0:1]], axis=2)[:, :, None, :]
    return jnp.concatenate([bottom, middle, top], axis=2)


def window(padded, shift_r, shift_c):
    patch_extent = padded.shape[2] - 2
    part = padded[
        :, :, 1 + shift_r : 1 + shift_r + patch_extent, 1 + shift_c : 1 + shift_c + patch_extent
    ]
    return part.reshape(padded.shape[0], padded.shape[1], patch_extent * patch_extent)


def conv_forward(padded, weights):
    total = None
    for k in range(9):
        term = jnp.einsum(
            "oi,tic->toc",
            weights[k],
            window(padded, k // 3 - 1, k % 3 - 1),
            preferred_element_type=jnp.float32,
        )
        total = term if total is None else total + term
    return total


def conv_adjoint(padded, weights):
    total = None
    for k in range(9):
        term = jnp.einsum(
            "oi,toc->tic",
            weights[k],
            window(padded, 1 - k // 3, 1 - k % 3),
            preferred_element_type=jnp.float32,
        )
        total = term if total is None else total + term
    return total


def weight_grad(grads, padded):
    return jnp.stack(
        [
            jnp.einsum(
                "toc,tic->oi",
                grads,
                window(padded, k // 3 - 1, k % 3 - 1),
                preferred_element_type=jnp.float32,
            )
            for k in range(9)
        ],
        axis=0,
    )


def halo_side_weight_grad(grad_padded, hidden_tiles, fold_flag):
    extent = hidden_tiles.shape[2]
    wide = jnp.pad(hidden_tiles, ((0, 0), (0, 0), (2, 2), (2, 2)))
    grads = grad_padded.reshape(grad_padded.shape[0], grad_padded.shape[1], -1)
    span = extent + 2
    terms = []
    for k in range(9):
        shift_r, shift_c = k // 3 - 1, k % 3 - 1
        part = wide[:, :, 1 + shift_r : 1 + shift_r + span, 1 + shift_c : 1 + shift_c + span]
        terms.append(
            jnp.einsum(
                "toc,tic->oi",
                grads,
                part.reshape(part.shape[0], part.shape[1], -1),
                preferred_element_type=jnp.float32,
            )
        )
    north = grad_padded[:, :, extent + 1, 1 : extent + 1]
    flipped = (fold_flag == 1).astype(jnp.float32)[:, None, None]
    for shift_c in (-1, 0, 1):
        segment = wide[:, :, extent + 1, 2 + shift_c : 2 + shift_c + extent]
        moved = jnp.einsum(
            "toc,tic->toi", north, segment, preferred_element_type=jnp.float32
        )
        moved = jnp.sum(moved * flipped, axis=0)
        terms[1 + shift_c] = terms[1 + shift_c] - moved
        terms[7 - shift_c] = terms[7 - shift_c] + moved
    return jnp.stack(terms, axis=0)


def body(input_states, loss_sensitivity, ocean, neighbours, fold_flag, w_first, w_second):
    tiles = input_states[0]
    patch_total, feature_depth, cells = tiles.shape
    patch_extent = SIDE
    inputs = tiles.reshape(patch_total, feature_depth, patch_extent, patch_extent)
    water_indicator = ocean.astype(jnp.float32)[:, None, :]
    masked_grad = (loss_sensitivity[0].astype(jnp.float32) * water_indicator).astype(jnp.bfloat16)
    grad_tiles = masked_grad.reshape(patch_total, feature_depth, patch_extent, patch_extent)
    field_parts, grad_parts = exchange_rims((inputs, grad_tiles), neighbours, fold_flag)
    in_padded = padded_tiles(inputs, field_parts)
    pre_first = conv_forward(in_padded, w_first)
    value, slope = gelu_pair(pre_first)
    hidden = (value * water_indicator).astype(jnp.bfloat16)
    hidden_tiles = hidden.reshape(patch_total, feature_depth, patch_extent, patch_extent)
    (hidden_parts,) = exchange_rims((hidden_tiles,), neighbours, fold_flag)
    hidden_padded = padded_tiles(hidden_tiles, hidden_parts)
    latter_linear_response = conv_forward(hidden_padded, w_second)
    prediction = (latter_linear_response * water_indicator).astype(jnp.bfloat16)[None]
    grad_padded = padded_tiles(grad_tiles, grad_parts)
    latter_kernel_slope = halo_side_weight_grad(grad_padded, hidden_tiles, fold_flag)
    back = conv_adjoint(grad_padded, w_second).reshape(
        patch_total, feature_depth, patch_extent, patch_extent
    )
    top_row = grad_padded[:, :, patch_extent + 1, :]
    correction = jnp.zeros((patch_total, feature_depth, patch_extent), jnp.float32)
    for shift_c in (-1, 0, 1):
        segment = top_row[:, :, 1 - shift_c : 1 - shift_c + patch_extent]
        correction = correction + jnp.einsum(
            "oi,toc->tic", w_second[7 - shift_c], segment, preferred_element_type=jnp.float32
        )
        correction = correction - jnp.einsum(
            "oi,toc->tic", w_second[1 + shift_c], segment, preferred_element_type=jnp.float32
        )
    flipped = (fold_flag == 1).astype(jnp.float32)[:, None, None]
    back = back.at[:, :, patch_extent - 1, :].add(correction * flipped)
    pre_grad = (back.reshape(patch_total, feature_depth, cells) * water_indicator * slope).astype(
        jnp.bfloat16
    )
    earlier_kernel_slope = weight_grad(pre_grad, in_padded)
    devices = lax.psum(1, REDUCE_AXES)
    earlier_kernel_slope = all_sum(earlier_kernel_slope, devices)
    latter_kernel_slope = all_sum(latter_kernel_slope, devices)
    return (prediction, earlier_kernel_slope, latter_kernel_slope)


def solution(mesh):
    placed = (
        P("dp", "space", None, None),
        P("dp", "space", None, None),
        P("space", None),
        P("space", None),
        P("space"),
        P(),
        P(),
    )
    return jax.shard_map(
        body,
        mesh=mesh,
        in_specs=placed,
        out_specs=(P("dp", "space", None, None), P(), P()),
        check_vma=False,
    )
```

```python
import jax
import jax.numpy as jnp
from jax import lax
from jax.sharding import PartitionSpec as P

SIDE = 32


SQRT_TWO_PI = 0.7978845608028654
CUBIC = 0.044715


def gelu_pair(a):
    inner = SQRT_TWO_PI * (a + CUBIC * a * a * a)
    tangent = jnp.tanh(inner)
    value = 0.5 * a * (1.0 + tangent)
    slope = 0.5 * (1.0 + tangent) + 0.5 * a * (1.0 - tangent * tangent) * SQRT_TWO_PI * (
        1.0 + 3.0 * CUBIC * a * a
    )
    return (value, slope)


def edge_strips(field):
    patch_extent = field.shape[2]
    return jnp.concatenate(
        [
            field[:, :, 0, :],
            field[:, :, patch_extent - 1, :],
            field[:, :, :, 0],
            field[:, :, :, patch_extent - 1],
        ],
        axis=2,
    )


def strip_parts(piece, neighbours, fold_flag):
    amount = piece.shape[0]
    patch_extent = piece.shape[2] // 4

    def pick(k):
        index = neighbours[:, k]
        valid = ((index >= 0) & (index < amount)).astype(piece.dtype)
        return jnp.take(piece, jnp.clip(index, 0, amount - 1), axis=0) * valid[:, None, None]

    from_north = pick(0)
    north = jnp.where(
        (fold_flag == 1)[:, None, None],
        from_north[:, :, patch_extent : 2 * patch_extent][:, :, ::-1],
        from_north[:, :, 0:patch_extent],
    )
    south = pick(1)[:, :, patch_extent : 2 * patch_extent]
    east = pick(2)[:, :, 2 * patch_extent : 3 * patch_extent]
    west = pick(3)[:, :, 3 * patch_extent : 4 * patch_extent]
    corners = jnp.stack(
        [
            pick(4)[:, :, 0],
            pick(5)[:, :, patch_extent - 1],
            pick(6)[:, :, patch_extent],
            pick(7)[:, :, 2 * patch_extent - 1],
        ],
        axis=-1,
    )
    return (north, south, east, west, corners)


def collect_rims(strips, neighbours, fold_flag):
    found = strip_parts(lax.all_gather(strips, "space", axis=0, tiled=True), neighbours, fold_flag)
    return tuple((b for b in found))


def collect_two_rims(first, second, neighbours, fold_flag):
    depth = first.shape[1]
    gathered = lax.all_gather(jnp.concatenate([first, second], axis=1), "space", axis=0, tiled=True)
    return (
        strip_parts(gathered[:, :depth], neighbours, fold_flag),
        strip_parts(gathered[:, depth:], neighbours, fold_flag),
    )


def exchange_rims(fields, neighbours, fold_flag):
    amount = lax.psum(1, "space")
    own = neighbours[0]
    dest = jnp.arange(amount, dtype=own.dtype)

    def toward(directions):
        hit = jnp.zeros((amount,), jnp.bool_)
        for k in directions:
            hit = hit | (own[k] == dest)
        return hit[:, None, None]

    up, down = toward((0, 4, 5)), toward((1, 6, 7))
    east, west = toward((2,)), toward((3,))
    slots = []
    for field in fields:
        extent = field.shape[2]
        row_low, row_high = field[0, :, 0, :], field[0, :, extent - 1, :]
        col_low, col_high = field[0, :, :, 0], field[0, :, :, extent - 1]
        empty = jnp.zeros_like(row_low)[None]
        slots.append(jnp.where(up, row_high[None], jnp.where(down, row_low[None], empty)))
        slots.append(jnp.where(east, col_high[None], jnp.where(west, col_low[None], empty)))
    got = lax.all_to_all(jnp.concatenate(slots, axis=2), "space", 0, 0, tiled=True)
    found = []
    for n, field in enumerate(fields):
        extent = field.shape[2]
        rows = got[:, :, 2 * n * extent : (2 * n + 1) * extent]
        cols = got[:, :, (2 * n + 1) * extent : (2 * n + 2) * extent]

        def pick(part, k):
            index = neighbours[:, k]
            valid = ((index >= 0) & (index < amount)).astype(part.dtype)
            return jnp.take(part, jnp.clip(index, 0, amount - 1), axis=0) * valid[:, None, None]

        from_north = pick(rows, 0)
        north = jnp.where((fold_flag == 1)[:, None, None], from_north[:, :, ::-1], from_north)
        corners = jnp.stack(
            [
                pick(rows, 4)[:, :, 0],
                pick(rows, 5)[:, :, extent - 1],
                pick(rows, 6)[:, :, 0],
                pick(rows, 7)[:, :, extent - 1],
            ],
            axis=-1,
        )
        found.append((north, pick(rows, 1), pick(cols, 2), pick(cols, 3), corners))
    return found


REDUCE_AXES = ("space", "dp")


def all_sum(x, mesh_sizes):
    n = mesh_sizes
    nbits = n.bit_length() - 1
    idx = lax.axis_index(REDUCE_AXES)
    buf = x.reshape(-1)
    size = buf.shape[0]
    padded = -(-size // n) * n
    buf = jnp.pad(buf, (0, padded - size))
    for b in range(nbits):
        half = buf.shape[0] // 2
        me = (idx >> b) & 1
        pairs = [(i, i ^ (1 << b)) for i in range(n)]
        keep = lax.dynamic_slice(buf, (me * half,), (half,))
        send = lax.dynamic_slice(buf, ((1 - me) * half,), (half,))
        buf = keep + lax.ppermute(send, REDUCE_AXES, pairs)
    for b in reversed(range(nbits)):
        me = (idx >> b) & 1
        pairs = [(i, i ^ (1 << b)) for i in range(n)]
        recv = lax.ppermute(buf, REDUCE_AXES, pairs)
        buf = jnp.concatenate([jnp.where(me == 0, buf, recv), jnp.where(me == 0, recv, buf)])
    return buf[:size].reshape(x.shape)


def padded_tiles(field, parts):
    north, south, east, west, corners = parts
    middle = jnp.concatenate([west[..., None], field, east[..., None]], axis=3)
    bottom = jnp.concatenate([corners[:, :, 3:4], south, corners[:, :, 2:3]], axis=2)[:, :, None, :]
    top = jnp.concatenate([corners[:, :, 1:2], north, corners[:, :, 0:1]], axis=2)[:, :, None, :]
    return jnp.concatenate([bottom, middle, top], axis=2)


def window(padded, shift_r, shift_c):
    patch_extent = padded.shape[2] - 2
    part = padded[
        :, :, 1 + shift_r : 1 + shift_r + patch_extent, 1 + shift_c : 1 + shift_c + patch_extent
    ]
    return part.reshape(padded.shape[0], padded.shape[1], patch_extent * patch_extent)


def conv_forward(padded, weights):
    total = None
    for k in range(9):
        term = jnp.einsum(
            "oi,tic->toc",
            weights[k],
            window(padded, k // 3 - 1, k % 3 - 1),
            preferred_element_type=jnp.float32,
        )
        total = term if total is None else total + term
    return total


def conv_adjoint(padded, weights):
    total = None
    for k in range(9):
        term = jnp.einsum(
            "oi,toc->tic",
            weights[k],
            window(padded, 1 - k // 3, 1 - k % 3),
            preferred_element_type=jnp.float32,
        )
        total = term if total is None else total + term
    return total


def weight_grad(grads, padded):
    return jnp.stack(
        [
            jnp.einsum(
                "toc,tic->oi",
                grads,
                window(padded, k // 3 - 1, k % 3 - 1),
                preferred_element_type=jnp.float32,
            )
            for k in range(9)
        ],
        axis=0,
    )


def halo_side_weight_grad(grad_padded, hidden_tiles, fold_flag):
    extent = hidden_tiles.shape[2]
    wide = jnp.pad(hidden_tiles, ((0, 0), (0, 0), (2, 2), (2, 2)))
    grads = grad_padded.reshape(grad_padded.shape[0], grad_padded.shape[1], -1)
    span = extent + 2
    terms = []
    for k in range(9):
        shift_r, shift_c = k // 3 - 1, k % 3 - 1
        part = wide[:, :, 1 + shift_r : 1 + shift_r + span, 1 + shift_c : 1 + shift_c + span]
        terms.append(
            jnp.einsum(
                "toc,tic->oi",
                grads,
                part.reshape(part.shape[0], part.shape[1], -1),
                preferred_element_type=jnp.float32,
            )
        )
    north = grad_padded[:, :, extent + 1, 1 : extent + 1]
    flipped = (fold_flag == 1).astype(jnp.float32)[:, None, None]
    for shift_c in (-1, 0, 1):
        segment = wide[:, :, extent + 1, 2 + shift_c : 2 + shift_c + extent]
        moved = jnp.einsum(
            "toc,tic->toi", north, segment, preferred_element_type=jnp.float32
        )
        moved = jnp.sum(moved * flipped, axis=0)
        terms[1 + shift_c] = terms[1 + shift_c] - moved
        terms[7 - shift_c] = terms[7 - shift_c] + moved
    return jnp.stack(terms, axis=0)


def body(input_states, loss_sensitivity, ocean, neighbours, fold_flag, w_first, w_second):
    tiles = input_states[0]
    patch_total, feature_depth, cells = tiles.shape
    patch_extent = SIDE
    inputs = tiles.reshape(patch_total, feature_depth, patch_extent, patch_extent)
    water_indicator = ocean.astype(jnp.float32)[:, None, :]
    masked_grad = (loss_sensitivity[0].astype(jnp.float32) * water_indicator).astype(jnp.bfloat16)
    grad_tiles = masked_grad.reshape(patch_total, feature_depth, patch_extent, patch_extent)
    field_parts, grad_parts = exchange_rims((inputs, grad_tiles), neighbours, fold_flag)
    in_padded = padded_tiles(inputs, field_parts)
    pre_first = conv_forward(in_padded, w_first)
    value, slope = gelu_pair(pre_first)
    hidden = (value * water_indicator).astype(jnp.bfloat16)
    hidden_tiles = hidden.reshape(patch_total, feature_depth, patch_extent, patch_extent)
    (hidden_parts,) = exchange_rims((hidden_tiles,), neighbours, fold_flag)
    hidden_padded = padded_tiles(hidden_tiles, hidden_parts)
    latter_linear_response = conv_forward(hidden_padded, w_second)
    prediction = (latter_linear_response * water_indicator).astype(jnp.bfloat16)[None]
    grad_padded = padded_tiles(grad_tiles, grad_parts)
    latter_kernel_slope = halo_side_weight_grad(grad_padded, hidden_tiles, fold_flag)
    back = conv_adjoint(grad_padded, w_second).reshape(
        patch_total, feature_depth, patch_extent, patch_extent
    )
    top_row = grad_padded[:, :, patch_extent + 1, :]
    correction = jnp.zeros((patch_total, feature_depth, patch_extent), jnp.float32)
    for shift_c in (-1, 0, 1):
        segment = top_row[:, :, 1 - shift_c : 1 - shift_c + patch_extent]
        correction = correction + jnp.einsum(
            "oi,toc->tic", w_second[7 - shift_c], segment, preferred_element_type=jnp.float32
        )
        correction = correction - jnp.einsum(
            "oi,toc->tic", w_second[1 + shift_c], segment, preferred_element_type=jnp.float32
        )
    flipped = (fold_flag == 1).astype(jnp.float32)[:, None, None]
    back = back.at[:, :, patch_extent - 1, :].add(correction * flipped)
    pre_grad = (back.reshape(patch_total, feature_depth, cells) * water_indicator * slope).astype(
        jnp.bfloat16
    )
    earlier_kernel_slope = weight_grad(pre_grad, in_padded)
    devices = lax.psum(1, REDUCE_AXES)
    both = all_sum(jnp.stack([earlier_kernel_slope, latter_kernel_slope]), devices)
    earlier_kernel_slope, latter_kernel_slope = both[0], both[1]
    return (prediction, earlier_kernel_slope, latter_kernel_slope)


def solution(mesh):
    placed = (
        P("dp", "space", None, None),
        P("dp", "space", None, None),
        P("space", None),
        P("space", None),
        P("space"),
        P(),
        P(),
    )
    return jax.shard_map(
        body,
        mesh=mesh,
        in_specs=placed,
        out_specs=(P("dp", "space", None, None), P(), P()),
        check_vma=False,
    )
```

```python
import jax
import jax.numpy as jnp
from jax import lax
from jax.sharding import PartitionSpec as P


SIDE = 32


SQRT_TWO_PI = 0.7978845608028654
CUBIC = 0.044715


def gelu_pair(a):
    inner = SQRT_TWO_PI * (a + CUBIC * a * a * a)
    tangent = jnp.tanh(inner)
    value = 0.5 * a * (1.0 + tangent)
    slope = 0.5 * (1.0 + tangent) + 0.5 * a * (1.0 - tangent * tangent) * SQRT_TWO_PI * (
        1.0 + 3.0 * CUBIC * a * a
    )
    return (value, slope)


def exchange_rims(fields, neighbours, fold_flag):
    amount = lax.psum(1, "space")
    own = neighbours[0]
    dest = jnp.arange(amount, dtype=own.dtype)

    def toward(directions):
        hit = jnp.zeros((amount,), jnp.bool_)
        for k in directions:
            hit = hit | (own[k] == dest)
        return hit[:, None, None]

    up, down = toward((0, 4, 5)), toward((1, 6, 7))
    east, west = toward((2,)), toward((3,))
    slots = []
    for field in fields:
        extent = field.shape[2]
        row_low, row_high = field[0, :, 0, :], field[0, :, extent - 1, :]
        col_low, col_high = field[0, :, :, 0], field[0, :, :, extent - 1]
        empty = jnp.zeros_like(row_low)[None]
        slots.append(jnp.where(up, row_high[None], jnp.where(down, row_low[None], empty)))
        slots.append(jnp.where(east, col_high[None], jnp.where(west, col_low[None], empty)))
    got = lax.all_to_all(jnp.concatenate(slots, axis=2), "space", 0, 0, tiled=True)
    found = []
    for n, field in enumerate(fields):
        extent = field.shape[2]
        rows = got[:, :, 2 * n * extent : (2 * n + 1) * extent]
        cols = got[:, :, (2 * n + 1) * extent : (2 * n + 2) * extent]

        def pick(part, k):
            index = neighbours[:, k]
            valid = ((index >= 0) & (index < amount)).astype(part.dtype)
            return jnp.take(part, jnp.clip(index, 0, amount - 1), axis=0) * valid[:, None, None]

        from_north = pick(rows, 0)
        north = jnp.where((fold_flag == 1)[:, None, None], from_north[:, :, ::-1], from_north)
        corners = jnp.stack(
            [
                pick(rows, 4)[:, :, 0],
                pick(rows, 5)[:, :, extent - 1],
                pick(rows, 6)[:, :, 0],
                pick(rows, 7)[:, :, extent - 1],
            ],
            axis=-1,
        )
        found.append((north, pick(rows, 1), pick(cols, 2), pick(cols, 3), corners))
    return found


REDUCE_AXES = ("space", "dp")


def bit_groups(devices):
    nbits = devices.bit_length() - 1
    groups = [[b] for b in range(min(3, nbits))]
    rest = list(range(len(groups), nbits))
    if len(rest) > 3:
        groups.append(rest[:-3])
        rest = rest[-3:]
    if rest:
        groups.append(rest)
    return groups


def all_sum(x, devices):
    idx = lax.axis_index(REDUCE_AXES)
    groups = bit_groups(devices)
    buf = x.reshape(-1)
    size = buf.shape[0]
    padded = -(-size // devices) * devices
    buf = jnp.pad(buf, (0, padded - size))

    def spread(j, bits):
        return sum(((j >> t) & 1) << b for t, b in enumerate(bits))

    def digit(bits):
        return sum(((idx >> b) & 1) << t for t, b in enumerate(bits))

    for bits in groups:
        radix = 1 << len(bits)
        piece = buf.shape[0] // radix
        mine = digit(bits)
        total = lax.dynamic_slice(buf, (mine * piece,), (piece,))
        for j in range(1, radix):
            pairs = [(i, i ^ spread(j, bits)) for i in range(devices)]
            sent = lax.dynamic_slice(buf, ((mine ^ j) * piece,), (piece,))
            total = total + lax.ppermute(sent, REDUCE_AXES, pairs)
        buf = total
    for bits in reversed(groups):
        radix = 1 << len(bits)
        mine = digit(bits)
        got = [buf]
        for j in range(1, radix):
            pairs = [(i, i ^ spread(j, bits)) for i in range(devices)]
            got.append(lax.ppermute(buf, REDUCE_AXES, pairs))
        parts = []
        for p in range(radix):
            rel = mine ^ p
            part = got[radix - 1]
            for j in range(radix - 2, -1, -1):
                part = jnp.where(rel == j, got[j], part)
            parts.append(part)
        buf = jnp.concatenate(parts)
    return buf[:size].reshape(x.shape)


def padded_tiles(field, parts):
    north, south, east, west, corners = parts
    middle = jnp.concatenate([west[..., None], field, east[..., None]], axis=3)
    bottom = jnp.concatenate([corners[:, :, 3:4], south, corners[:, :, 2:3]], axis=2)[:, :, None, :]
    top = jnp.concatenate([corners[:, :, 1:2], north, corners[:, :, 0:1]], axis=2)[:, :, None, :]
    return jnp.concatenate([bottom, middle, top], axis=2)


def window(padded, shift_r, shift_c):
    patch_extent = padded.shape[2] - 2
    part = padded[
        :, :, 1 + shift_r : 1 + shift_r + patch_extent, 1 + shift_c : 1 + shift_c + patch_extent
    ]
    return part.reshape(padded.shape[0], padded.shape[1], patch_extent * patch_extent)


def conv_forward(padded, weights):
    total = None
    for k in range(9):
        term = jnp.einsum(
            "oi,tic->toc",
            weights[k],
            window(padded, k // 3 - 1, k % 3 - 1),
            preferred_element_type=jnp.float32,
        )
        total = term if total is None else total + term
    return total


def conv_adjoint(padded, weights):
    total = None
    for k in range(9):
        term = jnp.einsum(
            "oi,toc->tic",
            weights[k],
            window(padded, 1 - k // 3, 1 - k % 3),
            preferred_element_type=jnp.float32,
        )
        total = term if total is None else total + term
    return total


def weight_grad(grads, padded):
    return jnp.stack(
        [
            jnp.einsum(
                "toc,tic->oi",
                grads,
                window(padded, k // 3 - 1, k % 3 - 1),
                preferred_element_type=jnp.float32,
            )
            for k in range(9)
        ],
        axis=0,
    )


def halo_side_weight_grad(grad_padded, hidden_tiles, fold_flag):
    extent = hidden_tiles.shape[2]
    wide = jnp.pad(hidden_tiles, ((0, 0), (0, 0), (2, 2), (2, 2)))
    grads = grad_padded.reshape(grad_padded.shape[0], grad_padded.shape[1], -1)
    span = extent + 2
    terms = []
    for k in range(9):
        shift_r, shift_c = k // 3 - 1, k % 3 - 1
        part = wide[:, :, 1 + shift_r : 1 + shift_r + span, 1 + shift_c : 1 + shift_c + span]
        terms.append(
            jnp.einsum(
                "toc,tic->oi",
                grads,
                part.reshape(part.shape[0], part.shape[1], -1),
                preferred_element_type=jnp.float32,
            )
        )
    north = grad_padded[:, :, extent + 1, 1 : extent + 1]
    flipped = (fold_flag == 1).astype(jnp.float32)[:, None, None]
    for shift_c in (-1, 0, 1):
        segment = wide[:, :, extent + 1, 2 + shift_c : 2 + shift_c + extent]
        moved = jnp.einsum(
            "toc,tic->toi", north, segment, preferred_element_type=jnp.float32
        )
        moved = jnp.sum(moved * flipped, axis=0)
        terms[1 + shift_c] = terms[1 + shift_c] - moved
        terms[7 - shift_c] = terms[7 - shift_c] + moved
    return jnp.stack(terms, axis=0)


def step_body(input_states, loss_sensitivity, ocean, neighbours, fold_flag, w_first, w_second):
    tiles = input_states[0]
    patch_total, feature_depth, cells = tiles.shape
    patch_extent = SIDE
    inputs = tiles.reshape(patch_total, feature_depth, patch_extent, patch_extent)
    water_indicator = ocean.astype(jnp.float32)[:, None, :]
    masked_grad = (loss_sensitivity[0].astype(jnp.float32) * water_indicator).astype(jnp.bfloat16)
    grad_tiles = masked_grad.reshape(patch_total, feature_depth, patch_extent, patch_extent)
    field_parts, grad_parts = exchange_rims((inputs, grad_tiles), neighbours, fold_flag)
    in_padded = padded_tiles(inputs, field_parts)
    pre_first = conv_forward(in_padded, w_first)
    value, slope = gelu_pair(pre_first)
    hidden = (value * water_indicator).astype(jnp.bfloat16)
    hidden_tiles = hidden.reshape(patch_total, feature_depth, patch_extent, patch_extent)
    (hidden_parts,) = exchange_rims((hidden_tiles,), neighbours, fold_flag)
    hidden_padded = padded_tiles(hidden_tiles, hidden_parts)
    latter_linear_response = conv_forward(hidden_padded, w_second)
    prediction = (latter_linear_response * water_indicator).astype(jnp.bfloat16)[None]
    grad_padded = padded_tiles(grad_tiles, grad_parts)
    latter_kernel_slope = halo_side_weight_grad(grad_padded, hidden_tiles, fold_flag)
    back = conv_adjoint(grad_padded, w_second).reshape(
        patch_total, feature_depth, patch_extent, patch_extent
    )
    top_row = grad_padded[:, :, patch_extent + 1, :]
    correction = jnp.zeros((patch_total, feature_depth, patch_extent), jnp.float32)
    for shift_c in (-1, 0, 1):
        segment = top_row[:, :, 1 - shift_c : 1 - shift_c + patch_extent]
        correction = correction + jnp.einsum(
            "oi,toc->tic", w_second[7 - shift_c], segment, preferred_element_type=jnp.float32
        )
        correction = correction - jnp.einsum(
            "oi,toc->tic", w_second[1 + shift_c], segment, preferred_element_type=jnp.float32
        )
    flipped = (fold_flag == 1).astype(jnp.float32)[:, None, None]
    back = back.at[:, :, patch_extent - 1, :].add(correction * flipped)
    pre_grad = (back.reshape(patch_total, feature_depth, cells) * water_indicator * slope).astype(
        jnp.bfloat16
    )
    earlier_kernel_slope = weight_grad(pre_grad, in_padded)
    devices = lax.psum(1, REDUCE_AXES)
    earlier_kernel_slope = all_sum(earlier_kernel_slope, devices)
    latter_kernel_slope = all_sum(latter_kernel_slope, devices)
    return (prediction, earlier_kernel_slope, latter_kernel_slope)


def solution(mesh):
    placed = (
        P("dp", "space", None, None),
        P("dp", "space", None, None),
        P("space", None),
        P("space", None),
        P("space"),
        P(),
        P(),
    )
    return jax.shard_map(
        step_body,
        mesh=mesh,
        in_specs=placed,
        out_specs=(P("dp", "space", None, None), P(), P()),
        check_vma=False,
    )
```

```python
import jax
import jax.numpy as jnp
from jax import lax
from jax.sharding import PartitionSpec as P


SIDE = 32


SQRT_TWO_PI = 0.7978845608028654
CUBIC = 0.044715


def gelu_pair(a):
    inner = SQRT_TWO_PI * (a + CUBIC * a * a * a)
    tangent = jnp.tanh(inner)
    value = 0.5 * a * (1.0 + tangent)
    slope = 0.5 * (1.0 + tangent) + 0.5 * a * (1.0 - tangent * tangent) * SQRT_TWO_PI * (
        1.0 + 3.0 * CUBIC * a * a
    )
    return (value, slope)


def exchange_rims(fields, neighbours, fold_flag):
    amount = lax.psum(1, "space")
    own = neighbours[0]
    dest = jnp.arange(amount, dtype=own.dtype)

    def toward(directions):
        hit = jnp.zeros((amount,), jnp.bool_)
        for k in directions:
            hit = hit | (own[k] == dest)
        return hit[:, None, None]

    up, down = toward((0, 4, 5)), toward((1, 6, 7))
    east, west = toward((2,)), toward((3,))
    slots = []
    for field in fields:
        extent = field.shape[2]
        row_low, row_high = field[0, :, 0, :], field[0, :, extent - 1, :]
        col_low, col_high = field[0, :, :, 0], field[0, :, :, extent - 1]
        empty = jnp.zeros_like(row_low)[None]
        slots.append(jnp.where(up, row_high[None], jnp.where(down, row_low[None], empty)))
        slots.append(jnp.where(east, col_high[None], jnp.where(west, col_low[None], empty)))
    got = lax.all_to_all(jnp.concatenate(slots, axis=2), "space", 0, 0, tiled=True)
    found = []
    for n, field in enumerate(fields):
        extent = field.shape[2]
        rows = got[:, :, 2 * n * extent : (2 * n + 1) * extent]
        cols = got[:, :, (2 * n + 1) * extent : (2 * n + 2) * extent]

        def pick(part, k):
            index = neighbours[:, k]
            valid = ((index >= 0) & (index < amount)).astype(part.dtype)
            return jnp.take(part, jnp.clip(index, 0, amount - 1), axis=0) * valid[:, None, None]

        from_north = pick(rows, 0)
        north = jnp.where((fold_flag == 1)[:, None, None], from_north[:, :, ::-1], from_north)
        corners = jnp.stack(
            [
                pick(rows, 4)[:, :, 0],
                pick(rows, 5)[:, :, extent - 1],
                pick(rows, 6)[:, :, 0],
                pick(rows, 7)[:, :, extent - 1],
            ],
            axis=-1,
        )
        found.append((north, pick(rows, 1), pick(cols, 2), pick(cols, 3), corners))
    return found


REDUCE_AXES = ("space", "dp")


def all_sum(x, mesh_sizes):
    n = mesh_sizes
    nbits = n.bit_length() - 1
    idx = lax.axis_index(REDUCE_AXES)
    buf = x.reshape(-1)
    size = buf.shape[0]
    padded = -(-size // n) * n
    buf = jnp.pad(buf, (0, padded - size))
    for b in range(nbits):
        half = buf.shape[0] // 2
        me = (idx >> b) & 1
        pairs = [(i, i ^ (1 << b)) for i in range(n)]
        keep = lax.dynamic_slice(buf, (me * half,), (half,))
        send = lax.dynamic_slice(buf, ((1 - me) * half,), (half,))
        buf = keep + lax.ppermute(send, REDUCE_AXES, pairs)
    for b in reversed(range(nbits)):
        me = (idx >> b) & 1
        pairs = [(i, i ^ (1 << b)) for i in range(n)]
        recv = lax.ppermute(buf, REDUCE_AXES, pairs)
        buf = jnp.concatenate([jnp.where(me == 0, buf, recv), jnp.where(me == 0, recv, buf)])
    return buf[:size].reshape(x.shape)


def padded_tiles(field, parts):
    north, south, east, west, corners = parts
    middle = jnp.concatenate([west[..., None], field, east[..., None]], axis=3)
    bottom = jnp.concatenate([corners[:, :, 3:4], south, corners[:, :, 2:3]], axis=2)[:, :, None, :]
    top = jnp.concatenate([corners[:, :, 1:2], north, corners[:, :, 0:1]], axis=2)[:, :, None, :]
    return jnp.concatenate([bottom, middle, top], axis=2)


def window(padded, shift_r, shift_c):
    patch_extent = padded.shape[2] - 2
    part = padded[
        :, :, 1 + shift_r : 1 + shift_r + patch_extent, 1 + shift_c : 1 + shift_c + patch_extent
    ]
    return part.reshape(padded.shape[0], padded.shape[1], patch_extent * patch_extent)


def conv_forward(padded, weights):
    total = None
    for k in range(9):
        term = jnp.einsum(
            "oi,tic->toc",
            weights[k],
            window(padded, k // 3 - 1, k % 3 - 1),
            preferred_element_type=jnp.float32,
        )
        total = term if total is None else total + term
    return total


def conv_adjoint(padded, weights):
    total = None
    for k in range(9):
        term = jnp.einsum(
            "oi,toc->tic",
            weights[k],
            window(padded, 1 - k // 3, 1 - k % 3),
            preferred_element_type=jnp.float32,
        )
        total = term if total is None else total + term
    return total


def weight_grad(grads, padded):
    return jnp.stack(
        [
            jnp.einsum(
                "toc,tic->oi",
                grads,
                window(padded, k // 3 - 1, k % 3 - 1),
                preferred_element_type=jnp.float32,
            )
            for k in range(9)
        ],
        axis=0,
    )


def halo_side_weight_grad(grad_padded, hidden_tiles, fold_flag):
    extent = hidden_tiles.shape[2]
    wide = jnp.pad(hidden_tiles, ((0, 0), (0, 0), (2, 2), (2, 2)))
    grads = grad_padded.reshape(grad_padded.shape[0], grad_padded.shape[1], -1)
    span = extent + 2
    terms = []
    for k in range(9):
        shift_r, shift_c = k // 3 - 1, k % 3 - 1
        part = wide[:, :, 1 + shift_r : 1 + shift_r + span, 1 + shift_c : 1 + shift_c + span]
        terms.append(
            jnp.einsum(
                "toc,tic->oi",
                grads,
                part.reshape(part.shape[0], part.shape[1], -1),
                preferred_element_type=jnp.float32,
            )
        )
    north = grad_padded[:, :, extent + 1, 1 : extent + 1]
    flipped = (fold_flag == 1).astype(jnp.float32)[:, None, None]
    for shift_c in (-1, 0, 1):
        segment = wide[:, :, extent + 1, 2 + shift_c : 2 + shift_c + extent]
        moved = jnp.einsum(
            "toc,tic->toi", north, segment, preferred_element_type=jnp.float32
        )
        moved = jnp.sum(moved * flipped, axis=0)
        terms[1 + shift_c] = terms[1 + shift_c] - moved
        terms[7 - shift_c] = terms[7 - shift_c] + moved
    return jnp.stack(terms, axis=0)


def step_body(input_states, loss_sensitivity, ocean, neighbours, fold_flag, w_first, w_second):
    tiles = input_states[0]
    patch_total, feature_depth, cells = tiles.shape
    patch_extent = SIDE
    inputs = tiles.reshape(patch_total, feature_depth, patch_extent, patch_extent)
    water_indicator = ocean.astype(jnp.float32)[:, None, :]
    masked_grad = (loss_sensitivity[0].astype(jnp.float32) * water_indicator).astype(jnp.bfloat16)
    grad_tiles = masked_grad.reshape(patch_total, feature_depth, patch_extent, patch_extent)
    field_parts, grad_parts = exchange_rims((inputs, grad_tiles), neighbours, fold_flag)
    in_padded = padded_tiles(inputs, field_parts)
    pre_first = conv_forward(in_padded, w_first)
    value, slope = gelu_pair(pre_first)
    hidden = (value * water_indicator).astype(jnp.bfloat16)
    hidden_tiles = hidden.reshape(patch_total, feature_depth, patch_extent, patch_extent)
    (hidden_parts,) = exchange_rims((hidden_tiles,), neighbours, fold_flag)
    hidden_padded = padded_tiles(hidden_tiles, hidden_parts)
    latter_linear_response = conv_forward(hidden_padded, w_second)
    prediction = (latter_linear_response * water_indicator).astype(jnp.bfloat16)[None]
    grad_padded = padded_tiles(grad_tiles, grad_parts)
    latter_kernel_slope = halo_side_weight_grad(grad_padded, hidden_tiles, fold_flag)
    back = conv_adjoint(grad_padded, w_second).reshape(
        patch_total, feature_depth, patch_extent, patch_extent
    )
    top_row = grad_padded[:, :, patch_extent + 1, :]
    correction = jnp.zeros((patch_total, feature_depth, patch_extent), jnp.float32)
    for shift_c in (-1, 0, 1):
        segment = top_row[:, :, 1 - shift_c : 1 - shift_c + patch_extent]
        correction = correction + jnp.einsum(
            "oi,toc->tic", w_second[7 - shift_c], segment, preferred_element_type=jnp.float32
        )
        correction = correction - jnp.einsum(
            "oi,toc->tic", w_second[1 + shift_c], segment, preferred_element_type=jnp.float32
        )
    flipped = (fold_flag == 1).astype(jnp.float32)[:, None, None]
    back = back.at[:, :, patch_extent - 1, :].add(correction * flipped)
    pre_grad = (back.reshape(patch_total, feature_depth, cells) * water_indicator * slope).astype(
        jnp.bfloat16
    )
    earlier_kernel_slope = weight_grad(pre_grad, in_padded)
    devices = lax.psum(1, REDUCE_AXES)
    earlier_kernel_slope = all_sum(earlier_kernel_slope, devices)
    latter_kernel_slope = all_sum(latter_kernel_slope, devices)
    return (prediction, earlier_kernel_slope, latter_kernel_slope)


def solution(mesh):
    placed = (
        P("dp", "space", None, None),
        P("dp", "space", None, None),
        P("space", None),
        P("space", None),
        P("space"),
        P(),
        P(),
    )
    return jax.shard_map(
        step_body,
        mesh=mesh,
        in_specs=placed,
        out_specs=(P("dp", "space", None, None), P(), P()),
        check_vma=False,
    )
```
